512 devices in a mesh: dp: 8 (over z_hi, core), seq: 64 (over x, z_lo, y).
Axes of the slice: x: 4, y: 8, z: 8 (z_hi: 4, z_lo: 2; z = z_hi * 2 + z_lo), core: 2. Of those that a mesh axis runs over, the one named last changes fastest.
Arguments:
- y_first: bfloat16 [8, 128, 64, 1152], P('dp', 'seq'), may hold values from -10 to 10
- y_second: bfloat16 [8, 128, 64, 1152], P('dp', 'seq'), may hold values from -10 to 10
- grad_first: bfloat16 [8, 128, 64, 1152], P('dp', 'seq'), may hold values from -6 to 6
- grad_second: bfloat16 [8, 128, 64, 1152], P('dp', 'seq'), may hold values from -6 to 6
- w_qkv_space: bfloat16 [1152, 1728], P('seq', 'dp'), may hold values from -1 to 1
- w_out_space: bfloat16 [576, 1152], P('seq', 'dp'), may hold values from -0.25 to 0.25
- w_qkv_time: bfloat16 [1152, 1728], P('seq', 'dp'), may hold values from -1 to 1
- w_out_time: bfloat16 [576, 1152], P('seq', 'dp'), may hold values from -0.25 to 0.25
Outputs:
- x_first: bfloat16 [8, 128, 64, 1152], P('dp', 'seq')
- x_second: bfloat16 [8, 128, 64, 1152], P('dp', 'seq')
- d_first: bfloat16 [8, 128, 64, 1152], P('dp', 'seq')
- d_second: bfloat16 [8, 128, 64, 1152], P('dp', 'seq')
- grad_w_out_time: float32 [576, 1152], P('seq', 'dp')
The draws below stay inside these ranges and needn't reach their ends.
All inputs are finite; a program needn't handle non-finite values.
Results may differ from the reference program's by a relative error of at most 0.025.
Values may be sent and summed in bfloat16 or wider, within the bound.
No kernel may reach another device: no remote copies, remote signals or barrier semaphores. Data moves between devices by JAX's collectives and lax.ppermute only.
A program may use at most 64 MiB of HBM per device.

```python
import math
import jax
import jax.numpy as jnp
from jax import lax

D = 1152
HEADS = 8
HD = 72
P_SIZE = 64
FRAMES = 128
CLIPS = 8


def base_tokens(key, salt):
    own = jax.random.fold_in(key, salt)
    return jnp.clip(jax.random.normal(jax.random.fold_in(own, 1), (CLIPS, FRAMES, P_SIZE, D), jnp.float32), -6.0, 6.0)


def base_weights(key, salt):
    own = jax.random.fold_in(key, salt)
    return jnp.clip(jax.random.normal(own, (D, 3 * HEADS * HD), jnp.float32), -4.0, 4.0) * D ** (-0.5)


def draw_y_first(key, part):
    tokens = base_tokens(key, 101)
    return tokens.astype(jnp.bfloat16)


def draw_y_second(key, part):
    tokens = base_tokens(key, 202)
    return tokens.astype(jnp.bfloat16)


def draw_w_qkv_space(key, part):
    weights = base_weights(key, 303)
    return weights.astype(jnp.bfloat16)


def draw_w_qkv_time(key, part):
    weights = base_weights(key, 404)
    return weights.astype(jnp.bfloat16)


def level_of(own_key, extent, split, least, top_value):
    def one(position, blocks):
        heights = jax.random.uniform(jax.random.fold_in(jax.random.fold_in(own_key, 6), position), (blocks,), jnp.float32, least / len(split), top_value / len(split))
        return jnp.repeat(jnp.exp(heights), extent[position] // blocks).reshape((-1,) + (1,) * (len(extent) - position - 1))

    level = one(*split[0])
    for cut in split[1:]:
        level = level * one(*cut)
    return level


def scatter_about(key, dims, deviation, bound, pieces=(), kind=jnp.bfloat16):
    entries = jax.random.normal(key, dims, jnp.float32) * deviation
    if len(pieces) > 0:
        entries = level_of(key, dims, pieces, -0.22, 0.18) * entries
    return jnp.clip(entries, min=-bound, max=bound).astype(kind)


def setup_inputs(seed: int = 0) -> dict:
    key_of = jax.random.split(jax.random.key(seed), 9)
    y_first = draw_y_first(jax.random.fold_in(key_of[8], 71), 0)
    y_second = draw_y_second(jax.random.fold_in(key_of[8], 71), 0)
    grad_first = scatter_about(key_of[2], (CLIPS, FRAMES, P_SIZE, D), 1.0, 6.0, ((0, 8), (1, 64)))
    grad_second = scatter_about(key_of[3], (CLIPS, FRAMES, P_SIZE, D), 1.0, 6.0, ((0, 8), (1, 64)))
    w_qkv_space = draw_w_qkv_space(jax.random.fold_in(key_of[8], 71), 0)
    w_out_space = scatter_about(key_of[5], (HEADS * HD, D), (HEADS * HD) ** -0.5, 0.25, ((0, 64), (1, 8)))
    w_qkv_time = draw_w_qkv_time(jax.random.fold_in(key_of[8], 71), 0)
    w_out_time = scatter_about(key_of[7], (HEADS * HD, D), (HEADS * HD) ** -0.5, 0.25, ((0, 64), (1, 8)))
    return {"y_first": y_first, "y_second": y_second, "grad_first": grad_first, "grad_second": grad_second, "w_qkv_space": w_qkv_space, "w_out_space": w_out_space, "w_qkv_time": w_qkv_time, "w_out_time": w_out_time}


def normalize(values):
    wide = values.astype(jnp.float32)
    scale = lax.rsqrt(lax.optimization_barrier(jnp.mean(wide * wide, axis=-1, keepdims=True)) + 1e-06)
    return (wide * scale).astype(jnp.bfloat16)

def attend(inputs, w_qkv, w_out):
    outer, rows, inner, width = inputs.shape
    normed = normalize(inputs).reshape(-1, width)
    packed = jnp.dot(normed, w_qkv, preferred_element_type=jnp.float32).astype(jnp.bfloat16)
    packed = packed.reshape(outer, rows, inner, 3, HEADS, HD)
    query = packed[:, :, :, 0]
    keys = packed[:, :, :, 1]
    values = packed[:, :, :, 2]
    scores = jnp.einsum('arbhk,asbhk->abhrs', query, keys, preferred_element_type=jnp.float32) / math.sqrt(HD)
    peak = lax.optimization_barrier(jnp.max(scores, axis=-1, keepdims=True))
    expo = jnp.exp(scores - peak)
    probs = (expo / lax.optimization_barrier(jnp.sum(expo, axis=-1, keepdims=True))).astype(jnp.bfloat16)
    mixed = jnp.einsum('abhrs,asbhk->arbhk', probs, values, preferred_element_type=jnp.float32).astype(jnp.bfloat16)
    mixed = mixed.reshape(outer, rows, inner, HEADS * HD)
    result = jnp.dot(mixed.reshape(-1, HEADS * HD), w_out, preferred_element_type=jnp.float32).astype(jnp.bfloat16)
    return (result.reshape(inputs.shape), mixed)

def reference(y_first, y_second, grad_first, grad_second, w_qkv_space, w_out_space, w_qkv_time, w_out_time):

    def one_clip(items):
        first, second, cot_first, cot_second = items

        def time_fn(inputs):
            return attend(inputs, w_qkv_time, w_out_time)

        def space_fn(inputs):
            return attend(inputs, w_qkv_space, w_out_space)[0]
        time_out, time_vjp, time_mixed = jax.vjp(time_fn, first[None], has_aux=True)
        second_in = (second.astype(jnp.float32) - time_out[0].astype(jnp.float32)).astype(jnp.bfloat16)
        space_out, space_vjp = jax.vjp(space_fn, second_in[:, :, None, :])
        first_in = (first.astype(jnp.float32) - space_out[:, :, 0].astype(jnp.float32)).astype(jnp.bfloat16)
        back_time = time_vjp(cot_second[None])[0]
        first_grad = (cot_first.astype(jnp.float32) + back_time[0].astype(jnp.float32)).astype(jnp.bfloat16)
        back_space = space_vjp(first_grad[:, :, None, :])[0]
        second_grad = (cot_second.astype(jnp.float32) + back_space[:, :, 0].astype(jnp.float32)).astype(jnp.bfloat16)
        partial_grad = lax.dot_general(time_mixed.reshape(-1, HEADS * HD), cot_second.reshape(-1, D), (((0,), (0,)), ((), ())), preferred_element_type=jnp.float32)
        return (first_in, second_in, first_grad, second_grad, partial_grad)
    first_in, second_in, first_grad, second_grad, partials = lax.map(one_clip, (y_first, y_second, grad_first, grad_second))
    return (first_in, second_in, first_grad, second_grad, lax.optimization_barrier(jnp.sum(partials, axis=0)))
```

```python
import math

import jax
import jax.numpy as jnp
from jax import lax
from jax.sharding import PartitionSpec as P

HEADS = 8
HD = 72


def for_sending(shard):

    def short(part):
        return part.astype(jnp.bfloat16) if part.dtype == jnp.float32 else part

    return jax.tree.map(short, shard)


def gather_weight(shard):
    rows, cols = shard.shape
    blocks = lax.all_gather(shard, ("dp", "seq"), axis=0, tiled=False)
    dp, seq = lax.axis_size("dp"), lax.axis_size("seq")
    blocks = blocks.reshape(dp, seq, rows, cols).transpose(1, 2, 0, 3)
    return blocks.reshape(seq * rows, dp * cols)


def scatter_grad(partial, dp, seq):
    rows, cols = partial.shape
    blocks = partial.reshape(seq, rows // seq, dp, cols // dp).transpose(2, 0, 1, 3)
    blocks = blocks.reshape(dp * seq * (rows // seq), cols // dp)
    return lax.psum_scatter(blocks, ("dp", "seq"), scatter_dimension=0, tiled=True)


def normalize(values):
    wide = values.astype(jnp.float32)
    scale = lax.rsqrt(jnp.mean(wide * wide, axis=-1, keepdims=True) + 1e-06)
    return (wide * scale).astype(jnp.bfloat16)


def attend(inputs, w_qkv, w_out):
    outer, rows, inner, width = inputs.shape
    normed = normalize(inputs).reshape(-1, width)
    packed = jnp.dot(normed, w_qkv, preferred_element_type=jnp.float32).astype(jnp.bfloat16)
    packed = packed.reshape(outer, rows, inner, 3, HEADS, HD)
    query = packed[:, :, :, 0]
    keys = packed[:, :, :, 1]
    values = packed[:, :, :, 2]
    scores = jnp.einsum(
        "arbhk,asbhk->abhrs", query, keys, preferred_element_type=jnp.float32
    ) / math.sqrt(HD)
    peak = jnp.max(scores, axis=-1, keepdims=True)
    expo = jnp.exp(scores - peak)
    probs = (expo / jnp.sum(expo, axis=-1, keepdims=True)).astype(jnp.bfloat16)
    mixed = jnp.einsum(
        "abhrs,asbhk->arbhk", probs, values, preferred_element_type=jnp.float32
    ).astype(jnp.bfloat16)
    mixed = mixed.reshape(outer, rows, inner, HEADS * HD)
    result = jnp.dot(
        mixed.reshape(-1, HEADS * HD), w_out, preferred_element_type=jnp.float32
    ).astype(jnp.bfloat16)
    return (result.reshape(inputs.shape), mixed)


def body(
    y_first, y_second, grad_first, grad_second, w_qkv_space, w_out_space, w_qkv_time, w_out_time
):
    space_qkv, space_proj, time_qkv, time_proj = (
        gather_weight(w) for w in (w_qkv_space, w_out_space, w_qkv_time, w_out_time)
    )
    frame_count = y_first.shape[1]
    tokens = y_first.shape[2]
    width = y_first.shape[3]

    def time_fn(inputs):
        return attend(inputs, time_qkv, time_proj)

    def space_fn(inputs):
        return attend(inputs, space_qkv, space_proj)[0]

    first_patch = lax.all_to_all(y_first, "seq", split_axis=2, concat_axis=1, tiled=True)
    time_out, time_vjp, time_mixed = jax.vjp(time_fn, first_patch, has_aux=True)
    time_frames = jax.tree.map(
        lambda part, own: part.astype(own.dtype),
        lax.all_to_all(for_sending(time_out), "seq", split_axis=1, concat_axis=2, tiled=True),
        time_out,
    )
    second_in = (y_second.astype(jnp.float32) - time_frames.astype(jnp.float32)).astype(
        jnp.bfloat16
    )
    space_out, space_vjp = jax.vjp(space_fn, second_in.reshape(frame_count, tokens, 1, width))
    first_in = (
        y_first.astype(jnp.float32) - space_out.reshape(y_first.shape).astype(jnp.float32)
    ).astype(jnp.bfloat16)
    cot_patch = lax.all_to_all(grad_second, "seq", split_axis=2, concat_axis=1, tiled=True)
    back_patch = time_vjp(cot_patch)[0]
    back_frames = jax.tree.map(
        lambda part, own: part.astype(own.dtype),
        lax.all_to_all(for_sending(back_patch), "seq", split_axis=1, concat_axis=2, tiled=True),
        back_patch,
    )
    first_grad = (grad_first.astype(jnp.float32) + back_frames.astype(jnp.float32)).astype(
        jnp.bfloat16
    )
    back_space = space_vjp(first_grad.reshape(frame_count, tokens, 1, width))[0]
    second_grad = (
        grad_second.astype(jnp.float32) + back_space.reshape(y_first.shape).astype(jnp.float32)
    ).astype(jnp.bfloat16)
    partial_grad = lax.dot_general(
        time_mixed.reshape(-1, time_mixed.shape[3]),
        cot_patch.reshape(-1, width),
        (((0,), (0,)), ((), ())),
        preferred_element_type=jnp.float32,
    )
    grad_share = scatter_grad(partial_grad, lax.axis_size("dp"), lax.axis_size("seq"))
    return (first_in, second_in, first_grad, second_grad, grad_share)


def solution(mesh):
    placed = (
        P("dp", "seq", None, None),
        P("dp", "seq", None, None),
        P("dp", "seq", None, None),
        P("dp", "seq", None, None),
        P("seq", "dp"),
        P("seq", "dp"),
        P("seq", "dp"),
        P("seq", "dp"),
    )
    return jax.shard_map(
        body,
        mesh=mesh,
        in_specs=placed,
        out_specs=(
            P("dp", "seq", None, None),
            P("dp", "seq", None, None),
            P("dp", "seq", None, None),
            P("dp", "seq", None, None),
            P("seq", "dp"),
        ),
        check_vma=False,
    )
```

```python
import math

import jax
import jax.numpy as jnp
from jax import lax
from jax.sharding import Mesh, PartitionSpec as P

HEADS = 8
HD = 72

DP = ("zh", "core")
SEQ = ("x", "zl", "y")


def gather_weight(shard):
    for axis, dim in (("core", 1), ("zh", 1), ("y", 0), ("zl", 0), ("x", 0)):
        shard = lax.all_gather(shard, axis, axis=dim, tiled=True)
    return shard


def scatter_grad(partial):
    rows, cols = partial.shape
    dp, seq = lax.axis_size(DP), lax.axis_size(SEQ)
    blocks = partial.reshape(seq, rows // seq, dp, cols // dp).transpose(2, 0, 1, 3)
    blocks = blocks.reshape(dp * seq, rows // seq, cols // dp)
    return lax.all_to_all(blocks, DP + SEQ, 0, 0, tiled=True).sum(0)


def for_sending(shard):

    def short(part):
        return part.astype(jnp.bfloat16) if part.dtype == jnp.float32 else part

    return jax.tree.map(short, shard)


def normalize(values):
    wide = values.astype(jnp.float32)
    scale = lax.rsqrt(jnp.mean(wide * wide, axis=-1, keepdims=True) + 1e-06)
    return (wide * scale).astype(jnp.bfloat16)


def attend(inputs, w_qkv, w_out):
    outer, rows, inner, width = inputs.shape
    normed = normalize(inputs).reshape(-1, width)
    packed = jnp.dot(normed, w_qkv, preferred_element_type=jnp.float32).astype(jnp.bfloat16)
    packed = packed.reshape(outer, rows, inner, 3, HEADS, HD)
    query = packed[:, :, :, 0]
    keys = packed[:, :, :, 1]
    values = packed[:, :, :, 2]
    scores = jnp.einsum(
        "arbhk,asbhk->abhrs", query, keys, preferred_element_type=jnp.float32
    ) / math.sqrt(HD)
    peak = jnp.max(scores, axis=-1, keepdims=True)
    expo = jnp.exp(scores - peak)
    probs = (expo / jnp.sum(expo, axis=-1, keepdims=True)).astype(jnp.bfloat16)
    mixed = jnp.einsum(
        "abhrs,asbhk->arbhk", probs, values, preferred_element_type=jnp.float32
    ).astype(jnp.bfloat16)
    mixed = mixed.reshape(outer, rows, inner, HEADS * HD)
    result = jnp.dot(
        mixed.reshape(-1, HEADS * HD), w_out, preferred_element_type=jnp.float32
    ).astype(jnp.bfloat16)
    return (result.reshape(inputs.shape), mixed)


def body(
    y_first, y_second, grad_first, grad_second, w_qkv_space, w_out_space, w_qkv_time, w_out_time
):
    space_qkv, space_proj, time_qkv, time_proj = (
        gather_weight(w) for w in (w_qkv_space, w_out_space, w_qkv_time, w_out_time)
    )
    frame_count = y_first.shape[1]
    tokens = y_first.shape[2]
    width = y_first.shape[3]

    def time_fn(inputs):
        return attend(inputs, time_qkv, time_proj)

    def space_fn(inputs):
        return attend(inputs, space_qkv, space_proj)[0]

    first_patch = lax.all_to_all(y_first, SEQ, split_axis=2, concat_axis=1, tiled=True)
    time_out, time_vjp, time_mixed = jax.vjp(time_fn, first_patch, has_aux=True)
    time_frames = jax.tree.map(
        lambda part, own: part.astype(own.dtype),
        lax.all_to_all(for_sending(time_out), SEQ, split_axis=1, concat_axis=2, tiled=True),
        time_out,
    )
    second_in = (y_second.astype(jnp.float32) - time_frames.astype(jnp.float32)).astype(
        jnp.bfloat16
    )
    space_out, space_vjp = jax.vjp(space_fn, second_in.reshape(frame_count, tokens, 1, width))
    first_in = (
        y_first.astype(jnp.float32) - space_out.reshape(y_first.shape).astype(jnp.float32)
    ).astype(jnp.bfloat16)
    cot_patch = lax.all_to_all(grad_second, SEQ, split_axis=2, concat_axis=1, tiled=True)
    back_patch = time_vjp(cot_patch)[0]
    back_frames = jax.tree.map(
        lambda part, own: part.astype(own.dtype),
        lax.all_to_all(for_sending(back_patch), SEQ, split_axis=1, concat_axis=2, tiled=True),
        back_patch,
    )
    first_grad = (grad_first.astype(jnp.float32) + back_frames.astype(jnp.float32)).astype(
        jnp.bfloat16
    )
    back_space = space_vjp(first_grad.reshape(frame_count, tokens, 1, width))[0]
    second_grad = (
        grad_second.astype(jnp.float32) + back_space.reshape(y_first.shape).astype(jnp.float32)
    ).astype(jnp.bfloat16)
    partial_grad = lax.dot_general(
        time_mixed.reshape(-1, time_mixed.shape[3]),
        cot_patch.reshape(-1, width),
        (((0,), (0,)), ((), ())),
        preferred_element_type=jnp.float32,
    )
    grad_share = scatter_grad(partial_grad)
    return (first_in, second_in, first_grad, second_grad, grad_share)


def solution(mesh):
    placed = (
        P(DP, SEQ, None, None),
        P(DP, SEQ, None, None),
        P(DP, SEQ, None, None),
        P(DP, SEQ, None, None),
        P(SEQ, DP),
        P(SEQ, DP),
        P(SEQ, DP),
        P(SEQ, DP),
    )
    dp, seq = mesh.devices.shape
    split = (dp // 2, 2, seq // 16, 2, 8)
    full = Mesh(mesh.devices.reshape(split), DP + SEQ)
    return jax.shard_map(
        body,
        mesh=full,
        in_specs=placed,
        out_specs=(
            P(DP, SEQ, None, None),
            P(DP, SEQ, None, None),
            P(DP, SEQ, None, None),
            P(DP, SEQ, None, None),
            P(SEQ, DP),
        ),
        check_vma=False,
    )
```

```python
import math

import jax
import jax.numpy as jnp
from jax import lax
from jax.sharding import Mesh, PartitionSpec as P

HEADS = 8
HD = 72

DP = ("zh", "core")
SEQ = ("x", "zl", "y")


def gather_weights(qkv_space, out_space, qkv_time, out_time):
    width = qkv_space.shape[1]
    pad = ((0, 0), (0, width - out_space.shape[1]))
    parts = (qkv_space, jnp.pad(out_space, pad), qkv_time, jnp.pad(out_time, pad))
    block = jnp.concatenate(parts, axis=0)
    for axis, dim in (("core", 1), ("zh", 1), ("y", 0), ("zl", 0), ("x", 0)):
        block = lax.all_gather(block, axis, axis=dim, tiled=True)
    dp, seq = lax.axis_size(DP), lax.axis_size(SEQ)
    block = block.reshape(seq, -1, dp * width)
    outs = []
    start = 0
    for shard, part in zip((qkv_space, out_space, qkv_time, out_time), parts):
        rows, cols = shard.shape
        piece = block[:, start:start + rows]
        start += rows
        piece = piece.reshape(seq * rows, dp, width)[:, :, :cols]
        outs.append(piece.reshape(seq * rows, dp * cols))
    return outs


def scatter_grad(partial):
    rows, cols = partial.shape
    dp, seq = lax.axis_size(DP), lax.axis_size(SEQ)
    blocks = partial.reshape(seq, rows // seq, dp, cols // dp).transpose(2, 0, 1, 3)
    blocks = blocks.reshape(dp * seq, rows // seq, cols // dp)
    sent = lax.all_to_all(blocks.astype(jnp.bfloat16), DP + SEQ, 0, 0, tiled=True)
    return sent.astype(jnp.float32).sum(0)


def for_sending(shard):

    def short(part):
        return part.astype(jnp.bfloat16) if part.dtype == jnp.float32 else part

    return jax.tree.map(short, shard)


def normalize(values):
    wide = values.astype(jnp.float32)
    scale = lax.rsqrt(jnp.mean(wide * wide, axis=-1, keepdims=True) + 1e-06)
    return (wide * scale).astype(jnp.bfloat16)


def attend(inputs, w_qkv, w_out):
    outer, rows, inner, width = inputs.shape
    normed = normalize(inputs).reshape(-1, width)
    packed = jnp.dot(normed, w_qkv, preferred_element_type=jnp.float32).astype(jnp.bfloat16)
    packed = packed.reshape(outer, rows, inner, 3, HEADS, HD)
    query = packed[:, :, :, 0]
    keys = packed[:, :, :, 1]
    values = packed[:, :, :, 2]
    scores = jnp.einsum(
        "arbhk,asbhk->abhrs", query, keys, preferred_element_type=jnp.float32
    ) / math.sqrt(HD)
    peak = jnp.max(scores, axis=-1, keepdims=True)
    expo = jnp.exp(scores - peak)
    probs = (expo / jnp.sum(expo, axis=-1, keepdims=True)).astype(jnp.bfloat16)
    mixed = jnp.einsum(
        "abhrs,asbhk->arbhk", probs, values, preferred_element_type=jnp.float32
    ).astype(jnp.bfloat16)
    mixed = mixed.reshape(outer, rows, inner, HEADS * HD)
    result = jnp.dot(
        mixed.reshape(-1, HEADS * HD), w_out, preferred_element_type=jnp.float32
    ).astype(jnp.bfloat16)
    return (result.reshape(inputs.shape), mixed)


def body(
    y_first, y_second, grad_first, grad_second, w_qkv_space, w_out_space, w_qkv_time, w_out_time
):
    space_qkv, space_proj, time_qkv, time_proj = gather_weights(
        w_qkv_space, w_out_space, w_qkv_time, w_out_time
    )
    frame_count = y_first.shape[1]
    tokens = y_first.shape[2]
    width = y_first.shape[3]

    def time_fn(inputs):
        return attend(inputs, time_qkv, time_proj)

    def space_fn(inputs):
        return attend(inputs, space_qkv, space_proj)[0]

    first_patch = lax.all_to_all(y_first, SEQ, split_axis=2, concat_axis=1, tiled=True)
    time_out, time_vjp, time_mixed = jax.vjp(time_fn, first_patch, has_aux=True)
    time_frames = jax.tree.map(
        lambda part, own: part.astype(own.dtype),
        lax.all_to_all(for_sending(time_out), SEQ, split_axis=1, concat_axis=2, tiled=True),
        time_out,
    )
    second_in = (y_second.astype(jnp.float32) - time_frames.astype(jnp.float32)).astype(
        jnp.bfloat16
    )
    space_out, space_vjp = jax.vjp(space_fn, second_in.reshape(frame_count, tokens, 1, width))
    first_in = (
        y_first.astype(jnp.float32) - space_out.reshape(y_first.shape).astype(jnp.float32)
    ).astype(jnp.bfloat16)
    cot_patch = lax.all_to_all(grad_second, SEQ, split_axis=2, concat_axis=1, tiled=True)
    back_patch = time_vjp(cot_patch)[0]
    back_frames = jax.tree.map(
        lambda part, own: part.astype(own.dtype),
        lax.all_to_all(for_sending(back_patch), SEQ, split_axis=1, concat_axis=2, tiled=True),
        back_patch,
    )
    first_grad = (grad_first.astype(jnp.float32) + back_frames.astype(jnp.float32)).astype(
        jnp.bfloat16
    )
    back_space = space_vjp(first_grad.reshape(frame_count, tokens, 1, width))[0]
    second_grad = (
        grad_second.astype(jnp.float32) + back_space.reshape(y_first.shape).astype(jnp.float32)
    ).astype(jnp.bfloat16)
    partial_grad = lax.dot_general(
        time_mixed.reshape(-1, time_mixed.shape[3]),
        cot_patch.reshape(-1, width),
        (((0,), (0,)), ((), ())),
        preferred_element_type=jnp.float32,
    )
    grad_share = scatter_grad(partial_grad)
    return (first_in, second_in, first_grad, second_grad, grad_share)


def solution(mesh):
    placed = (
        P(DP, SEQ, None, None),
        P(DP, SEQ, None, None),
        P(DP, SEQ, None, None),
        P(DP, SEQ, None, None),
        P(SEQ, DP),
        P(SEQ, DP),
        P(SEQ, DP),
        P(SEQ, DP),
    )
    dp, seq = mesh.devices.shape
    split = (dp // 2, 2, seq // 16, 2, 8)
    full = Mesh(mesh.devices.reshape(split), DP + SEQ)
    return jax.shard_map(
        body,
        mesh=full,
        in_specs=placed,
        out_specs=(
            P(DP, SEQ, None, None),
            P(DP, SEQ, None, None),
            P(DP, SEQ, None, None),
            P(DP, SEQ, None, None),
            P(SEQ, DP),
        ),
        check_vma=False,
    )
```

```python
import math

import jax
import jax.numpy as jnp
from jax import lax
from jax.sharding import Mesh, PartitionSpec as P

HEADS = 8
HD = 72

DP = ("zh", "core")
SEQ = ("x", "zl", "y")


def gather_weight(shard):
    for axis, dim in (("core", 1), ("zh", 1), ("y", 0), ("zl", 0), ("x", 0)):
        shard = lax.all_gather(shard, axis, axis=dim, tiled=True)
    return shard


def scatter_grad(partial):
    rows, cols = partial.shape
    dp, seq = lax.axis_size(DP), lax.axis_size(SEQ)
    blocks = partial.reshape(seq, rows // seq, dp, cols // dp).transpose(2, 0, 1, 3)
    blocks = blocks.reshape(dp * seq, rows // seq, cols // dp)
    sent = lax.all_to_all(blocks.astype(jnp.bfloat16), DP + SEQ, 0, 0, tiled=True)
    return sent.astype(jnp.float32).sum(0)


def for_sending(shard):

    def short(part):
        return part.astype(jnp.bfloat16) if part.dtype == jnp.float32 else part

    return jax.tree.map(short, shard)


def normalize(values):
    wide = values.astype(jnp.float32)
    scale = lax.rsqrt(jnp.mean(wide * wide, axis=-1, keepdims=True) + 1e-06)
    return (wide * scale).astype(jnp.bfloat16)


def attend(inputs, w_qkv, w_out):
    outer, rows, inner, width = inputs.shape
    normed = normalize(inputs).reshape(-1, width)
    packed = jnp.dot(normed, w_qkv, preferred_element_type=jnp.float32).astype(jnp.bfloat16)
    packed = packed.reshape(outer, rows, inner, 3, HEADS, HD)
    query = packed[:, :, :, 0]
    keys = packed[:, :, :, 1]
    values = packed[:, :, :, 2]
    scores = jnp.einsum(
        "arbhk,asbhk->abhrs", query, keys, preferred_element_type=jnp.float32
    ) / math.sqrt(HD)
    peak = jnp.max(scores, axis=-1, keepdims=True)
    expo = jnp.exp(scores - peak)
    probs = (expo / jnp.sum(expo, axis=-1, keepdims=True)).astype(jnp.bfloat16)
    mixed = jnp.einsum(
        "abhrs,asbhk->arbhk", probs, values, preferred_element_type=jnp.float32
    ).astype(jnp.bfloat16)
    mixed = mixed.reshape(outer, rows, inner, HEADS * HD)
    result = jnp.dot(
        mixed.reshape(-1, HEADS * HD), w_out, preferred_element_type=jnp.float32
    ).astype(jnp.bfloat16)
    return (result.reshape(inputs.shape), mixed)


def body(
    y_first, y_second, grad_first, grad_second, w_qkv_space, w_out_space, w_qkv_time, w_out_time
):
    time_qkv, time_proj, space_qkv, space_proj = (
        gather_weight(w) for w in (w_qkv_time, w_out_time, w_qkv_space, w_out_space)
    )
    frame_count = y_first.shape[1]
    tokens = y_first.shape[2]
    width = y_first.shape[3]

    def time_fn(inputs):
        return attend(inputs, time_qkv, time_proj)

    def space_fn(inputs):
        return attend(inputs, space_qkv, space_proj)[0]

    first_patch = lax.all_to_all(y_first, SEQ, split_axis=2, concat_axis=1, tiled=True)
    time_out, time_vjp, time_mixed = jax.vjp(time_fn, first_patch, has_aux=True)
    time_frames = jax.tree.map(
        lambda part, own: part.astype(own.dtype),
        lax.all_to_all(for_sending(time_out), SEQ, split_axis=1, concat_axis=2, tiled=True),
        time_out,
    )
    second_in = (y_second.astype(jnp.float32) - time_frames.astype(jnp.float32)).astype(
        jnp.bfloat16
    )
    space_out, space_vjp = jax.vjp(space_fn, second_in.reshape(frame_count, tokens, 1, width))
    first_in = (
        y_first.astype(jnp.float32) - space_out.reshape(y_first.shape).astype(jnp.float32)
    ).astype(jnp.bfloat16)
    cot_patch = lax.all_to_all(grad_second, SEQ, split_axis=2, concat_axis=1, tiled=True)
    back_patch = time_vjp(cot_patch)[0]
    back_frames = jax.tree.map(
        lambda part, own: part.astype(own.dtype),
        lax.all_to_all(for_sending(back_patch), SEQ, split_axis=1, concat_axis=2, tiled=True),
        back_patch,
    )
    first_grad = (grad_first.astype(jnp.float32) + back_frames.astype(jnp.float32)).astype(
        jnp.bfloat16
    )
    back_space = space_vjp(first_grad.reshape(frame_count, tokens, 1, width))[0]
    second_grad = (
        grad_second.astype(jnp.float32) + back_space.reshape(y_first.shape).astype(jnp.float32)
    ).astype(jnp.bfloat16)
    partial_grad = lax.dot_general(
        time_mixed.reshape(-1, time_mixed.shape[3]),
        cot_patch.reshape(-1, width),
        (((0,), (0,)), ((), ())),
        preferred_element_type=jnp.float32,
    )
    grad_share = scatter_grad(partial_grad)
    return (first_in, second_in, first_grad, second_grad, grad_share)


def solution(mesh):
    placed = (
        P(DP, SEQ, None, None),
        P(DP, SEQ, None, None),
        P(DP, SEQ, None, None),
        P(DP, SEQ, None, None),
        P(SEQ, DP),
        P(SEQ, DP),
        P(SEQ, DP),
        P(SEQ, DP),
    )
    dp, seq = mesh.devices.shape
    split = (dp // 2, 2, seq // 16, 2, 8)
    full = Mesh(mesh.devices.reshape(split), DP + SEQ)
    return jax.shard_map(
        body,
        mesh=full,
        in_specs=placed,
        out_specs=(
            P(DP, SEQ, None, None),
            P(DP, SEQ, None, None),
            P(DP, SEQ, None, None),
            P(DP, SEQ, None, None),
            P(SEQ, DP),
        ),
        check_vma=False,
    )
```

```python
import math

import jax
import jax.numpy as jnp
from jax import lax
from jax.sharding import Mesh, PartitionSpec as P

HEADS = 8
HD = 72

DP = ("zh", "core")
SEQ = ("x", "zl", "y")


def gather_weight(shard):
    for axis, dim in ((DP, 1), ("y", 0), (("x", "zl"), 0)):
        shard = lax.all_gather(shard, axis, axis=dim, tiled=True)
    return shard


def scatter_grad(partial):
    rows, cols = partial.shape
    dp, seq = lax.axis_size(DP), lax.axis_size(SEQ)
    blocks = partial.reshape(seq, rows // seq, dp, cols // dp).transpose(2, 0, 1, 3)
    blocks = blocks.reshape(dp * seq, rows // seq, cols // dp)
    sent = lax.all_to_all(blocks.astype(jnp.bfloat16), DP + SEQ, 0, 0, tiled=True)
    return sent.astype(jnp.float32).sum(0)


def for_sending(shard):

    def short(part):
        return part.astype(jnp.bfloat16) if part.dtype == jnp.float32 else part

    return jax.tree.map(short, shard)


def normalize(values):
    wide = values.astype(jnp.float32)
    scale = lax.rsqrt(jnp.mean(wide * wide, axis=-1, keepdims=True) + 1e-06)
    return (wide * scale).astype(jnp.bfloat16)


def attend(inputs, w_qkv, w_out):
    outer, rows, inner, width = inputs.shape
    normed = normalize(inputs).reshape(-1, width)
    packed = jnp.dot(normed, w_qkv, preferred_element_type=jnp.float32).astype(jnp.bfloat16)
    packed = packed.reshape(outer, rows, inner, 3, HEADS, HD)
    query = packed[:, :, :, 0]
    keys = packed[:, :, :, 1]
    values = packed[:, :, :, 2]
    scores = jnp.einsum(
        "arbhk,asbhk->abhrs", query, keys, preferred_element_type=jnp.float32
    ) / math.sqrt(HD)
    peak = jnp.max(scores, axis=-1, keepdims=True)
    expo = jnp.exp(scores - peak)
    probs = (expo / jnp.sum(expo, axis=-1, keepdims=True)).astype(jnp.bfloat16)
    mixed = jnp.einsum(
        "abhrs,asbhk->arbhk", probs, values, preferred_element_type=jnp.float32
    ).astype(jnp.bfloat16)
    mixed = mixed.reshape(outer, rows, inner, HEADS * HD)
    result = jnp.dot(
        mixed.reshape(-1, HEADS * HD), w_out, preferred_element_type=jnp.float32
    ).astype(jnp.bfloat16)
    return (result.reshape(inputs.shape), mixed)


def body(
    y_first, y_second, grad_first, grad_second, w_qkv_space, w_out_space, w_qkv_time, w_out_time
):
    time_qkv, time_proj, space_qkv, space_proj = (
        gather_weight(w) for w in (w_qkv_time, w_out_time, w_qkv_space, w_out_space)
    )
    frame_count = y_first.shape[1]
    tokens = y_first.shape[2]
    width = y_first.shape[3]

    def time_fn(inputs):
        return attend(inputs, time_qkv, time_proj)

    def space_fn(inputs):
        return attend(inputs, space_qkv, space_proj)[0]

    first_patch = lax.all_to_all(y_first, SEQ, split_axis=2, concat_axis=1, tiled=True)
    time_out, time_vjp, time_mixed = jax.vjp(time_fn, first_patch, has_aux=True)
    time_frames = jax.tree.map(
        lambda part, own: part.astype(own.dtype),
        lax.all_to_all(for_sending(time_out), SEQ, split_axis=1, concat_axis=2, tiled=True),
        time_out,
    )
    second_in = (y_second.astype(jnp.float32) - time_frames.astype(jnp.float32)).astype(
        jnp.bfloat16
    )
    space_out, space_vjp = jax.vjp(space_fn, second_in.reshape(frame_count, tokens, 1, width))
    first_in = (
        y_first.astype(jnp.float32) - space_out.reshape(y_first.shape).astype(jnp.float32)
    ).astype(jnp.bfloat16)
    cot_patch = lax.all_to_all(grad_second, SEQ, split_axis=2, concat_axis=1, tiled=True)
    back_patch = time_vjp(cot_patch)[0]
    back_frames = jax.tree.map(
        lambda part, own: part.astype(own.dtype),
        lax.all_to_all(for_sending(back_patch), SEQ, split_axis=1, concat_axis=2, tiled=True),
        back_patch,
    )
    first_grad = (grad_first.astype(jnp.float32) + back_frames.astype(jnp.float32)).astype(
        jnp.bfloat16
    )
    back_space = space_vjp(first_grad.reshape(frame_count, tokens, 1, width))[0]
    second_grad = (
        grad_second.astype(jnp.float32) + back_space.reshape(y_first.shape).astype(jnp.float32)
    ).astype(jnp.bfloat16)
    partial_grad = lax.dot_general(
        time_mixed.reshape(-1, time_mixed.shape[3]),
        cot_patch.reshape(-1, width),
        (((0,), (0,)), ((), ())),
        preferred_element_type=jnp.float32,
    )
    grad_share = scatter_grad(partial_grad)
    return (first_in, second_in, first_grad, second_grad, grad_share)


def solution(mesh):
    placed = (
        P(DP, SEQ, None, None),
        P(DP, SEQ, None, None),
        P(DP, SEQ, None, None),
        P(DP, SEQ, None, None),
        P(SEQ, DP),
        P(SEQ, DP),
        P(SEQ, DP),
        P(SEQ, DP),
    )
    dp, seq = mesh.devices.shape
    split = (dp // 2, 2, seq // 16, 2, 8)
    full = Mesh(mesh.devices.reshape(split), DP + SEQ)
    return jax.shard_map(
        body,
        mesh=full,
        in_specs=placed,
        out_specs=(
            P(DP, SEQ, None, None),
            P(DP, SEQ, None, None),
            P(DP, SEQ, None, None),
            P(DP, SEQ, None, None),
            P(SEQ, DP),
        ),
        check_vma=False,
    )
```

```python
import math

import jax
import jax.numpy as jnp
from jax import lax
from jax.sharding import Mesh, PartitionSpec as P

HEADS = 8
HD = 72

DP = ("zh", "core")
SEQ = ("x", "zl", "y")


def gather_weight(shard):
    for axis, dim in (("core", 1), ("zh", 1), ("y", 0), ("zl", 0), ("x", 0)):
        shard = lax.all_gather(shard, axis, axis=dim, tiled=True)
    return shard


def scatter_grad(mixed, cot):
    dp, seq = lax.axis_size(DP), lax.axis_size(SEQ)
    mixed = mixed.reshape(-1, seq, mixed.shape[-1] // seq)
    cot = cot.reshape(-1, dp, cot.shape[-1] // dp)
    blocks = jnp.einsum("tsr,tdc->dsrc", mixed, cot, preferred_element_type=jnp.float32)
    blocks = blocks.reshape(dp * seq, mixed.shape[-1], cot.shape[-1])
    sent = lax.all_to_all(blocks.astype(jnp.bfloat16), DP + SEQ, 0, 0, tiled=True)
    return sent.astype(jnp.float32).sum(0)


def for_sending(shard):

    def short(part):
        return part.astype(jnp.bfloat16) if part.dtype == jnp.float32 else part

    return jax.tree.map(short, shard)


def normalize(values):
    wide = values.astype(jnp.float32)
    scale = lax.rsqrt(jnp.mean(wide * wide, axis=-1, keepdims=True) + 1e-06)
    return (wide * scale).astype(jnp.bfloat16)


def attend(inputs, w_qkv, w_out):
    outer, rows, inner, width = inputs.shape
    normed = normalize(inputs).reshape(-1, width)
    packed = jnp.dot(normed, w_qkv, preferred_element_type=jnp.float32).astype(jnp.bfloat16)
    packed = packed.reshape(outer, rows, inner, 3, HEADS, HD)
    query = packed[:, :, :, 0]
    keys = packed[:, :, :, 1]
    values = packed[:, :, :, 2]
    scores = jnp.einsum(
        "arbhk,asbhk->abhrs", query, keys, preferred_element_type=jnp.float32
    ) / math.sqrt(HD)
    peak = jnp.max(scores, axis=-1, keepdims=True)
    expo = jnp.exp(scores - peak)
    probs = (expo / jnp.sum(expo, axis=-1, keepdims=True)).astype(jnp.bfloat16)
    mixed = jnp.einsum(
        "abhrs,asbhk->arbhk", probs, values, preferred_element_type=jnp.float32
    ).astype(jnp.bfloat16)
    mixed = mixed.reshape(outer, rows, inner, HEADS * HD)
    result = jnp.dot(
        mixed.reshape(-1, HEADS * HD), w_out, preferred_element_type=jnp.float32
    ).astype(jnp.bfloat16)
    return (result.reshape(inputs.shape), mixed)


def body(
    y_first, y_second, grad_first, grad_second, w_qkv_space, w_out_space, w_qkv_time, w_out_time
):
    time_qkv, time_proj, space_qkv, space_proj = (
        gather_weight(w) for w in (w_qkv_time, w_out_time, w_qkv_space, w_out_space)
    )
    frame_count = y_first.shape[1]
    tokens = y_first.shape[2]
    width = y_first.shape[3]

    def time_fn(inputs):
        return attend(inputs, time_qkv, time_proj)

    def space_fn(inputs):
        return attend(inputs, space_qkv, space_proj)[0]

    first_patch = lax.all_to_all(y_first, SEQ, split_axis=2, concat_axis=1, tiled=True)
    time_out, time_vjp, time_mixed = jax.vjp(time_fn, first_patch, has_aux=True)
    time_frames = jax.tree.map(
        lambda part, own: part.astype(own.dtype),
        lax.all_to_all(for_sending(time_out), SEQ, split_axis=1, concat_axis=2, tiled=True),
        time_out,
    )
    second_in = (y_second.astype(jnp.float32) - time_frames.astype(jnp.float32)).astype(
        jnp.bfloat16
    )
    space_out, space_vjp = jax.vjp(space_fn, second_in.reshape(frame_count, tokens, 1, width))
    first_in = (
        y_first.astype(jnp.float32) - space_out.reshape(y_first.shape).astype(jnp.float32)
    ).astype(jnp.bfloat16)
    cot_patch = lax.all_to_all(grad_second, SEQ, split_axis=2, concat_axis=1, tiled=True)
    back_patch = time_vjp(cot_patch)[0]
    back_frames = jax.tree.map(
        lambda part, own: part.astype(own.dtype),
        lax.all_to_all(for_sending(back_patch), SEQ, split_axis=1, concat_axis=2, tiled=True),
        back_patch,
    )
    first_grad = (grad_first.astype(jnp.float32) + back_frames.astype(jnp.float32)).astype(
        jnp.bfloat16
    )
    back_space = space_vjp(first_grad.reshape(frame_count, tokens, 1, width))[0]
    second_grad = (
        grad_second.astype(jnp.float32) + back_space.reshape(y_first.shape).astype(jnp.float32)
    ).astype(jnp.bfloat16)
    grad_share = scatter_grad(
        time_mixed.reshape(-1, time_mixed.shape[3]), cot_patch.reshape(-1, width)
    )
    return (first_in, second_in, first_grad, second_grad, grad_share)


def solution(mesh):
    placed = (
        P(DP, SEQ, None, None),
        P(DP, SEQ, None, None),
        P(DP, SEQ, None, None),
        P(DP, SEQ, None, None),
        P(SEQ, DP),
        P(SEQ, DP),
        P(SEQ, DP),
        P(SEQ, DP),
    )
    dp, seq = mesh.devices.shape
    split = (dp // 2, 2, seq // 16, 2, 8)
    full = Mesh(mesh.devices.reshape(split), DP + SEQ)
    return jax.shard_map(
        body,
        mesh=full,
        in_specs=placed,
        out_specs=(
            P(DP, SEQ, None, None),
            P(DP, SEQ, None, None),
            P(DP, SEQ, None, None),
            P(DP, SEQ, None, None),
            P(SEQ, DP),
        ),
        check_vma=False,
    )
```
